32 devices in a mesh: row: 4 (over y, x), col: 8 (over z, core).
Axes of the slice: x: 2, y: 2, z: 4, core: 2. Of those that a mesh axis runs over, the one named last changes fastest.
Arguments:
- covariance: float32 [20, 4, 10, 8, 256, 256], P(None, 'row', None, 'col'), may hold values from -0.006 to 2.4, as said below
- telemetry: bfloat16 [1536, 10, 8, 256], P('row', None, 'col'), may hold values from -6 to 6
- active: int32 [8, 1280], replicated, may hold values 0 or 1
- panel: int32 [1], replicated, may hold values from 0 to 75
Outputs:
- factored: float32 [20, 4, 10, 8, 256, 256], P(None, 'row', None, 'col')
The draws below stay inside these ranges and needn't reach their ends.
Inputs may be any that keep to these rules, and one draw needn't show every extreme that they name: `covariance`: in every diagonal tile each diagonal entry exceeds the sum of magnitudes of the other entries of its row; entries off the matrix diagonal lie in -0.006 to 0.006.
All inputs are finite; a program needn't handle non-finite values.
Results may differ from the reference program's by a relative error of at most 0.0006.
Values may be sent and summed in bfloat16 or wider, within the bound.
No kernel may reach another device: no remote copies, remote signals or barrier semaphores. Data moves between devices by JAX's collectives and lax.ppermute only.
A program may use at most 384 MiB of HBM per device.

```python
import jax
import jax.numpy as jnp
from jax import lax

SENS = 8
SUBAP = 1280
TB = 256
SAMPLES = 1536
TILES = 80
N_ROW = 4
N_COL = 8


def draw_covariance(key, part):
    key_offdiag = jax.random.fold_in(key, 11)
    key_diagonal = jax.random.fold_in(key, 12)
    offdiag = jax.random.uniform(key_offdiag, (TILES, TILES, TB, TB), jnp.float32, -0.006, 0.006)
    diagonal = jax.random.uniform(key_diagonal, (TILES, TB), jnp.float32, 1.7, 2.3)
    same_tile = (jnp.arange(TILES)[:, None] == jnp.arange(TILES)[None, :])[:, :, None, None]
    same_cell = (jnp.arange(TB)[:, None] == jnp.arange(TB)[None, :])[None, None, :, :]
    values = jnp.where(same_tile & same_cell, diagonal[:, None, :, None], offdiag)
    return values.reshape(TILES // N_ROW, N_ROW, TILES // N_COL, N_COL, TB, TB)


def set_ends(values, own_key, least, high):
    place = [jax.random.randint(jax.random.fold_in(own_key, axis), (), 0, length) for axis, length in enumerate(values.shape)]
    main_axis = values.shape.index(max(values.shape))
    next_to = place[:main_axis] + [(place[main_axis] + 1) % values.shape[main_axis]] + place[main_axis + 1:]
    return values.at[tuple(place)].set(least).at[tuple(next_to)].set(high)


def shard_levels(key, extent, pieces, least, largest):
    def one(axis_at, shards_of):
        heights = jax.random.uniform(jax.random.fold_in(jax.random.fold_in(key, 6), axis_at), (shards_of,), jnp.float32, least / len(pieces), largest / len(pieces))
        return jnp.repeat(jnp.exp(heights), extent[axis_at] // shards_of).reshape((-1,) + (1,) * (len(extent) - axis_at - 1))

    factor_of = one(*pieces[0])
    for cut in pieces[1:]:
        factor_of = factor_of * one(*cut)
    return factor_of


def scatter_about(rng, shape, deviation, most, pieces=(), held_as=jnp.bfloat16):
    loudness = shard_levels(rng, shape, pieces, -0.22, 0.18) if pieces else 1.0
    entries = jax.random.normal(rng, shape, jnp.float32) * deviation * loudness
    return jnp.minimum(jnp.maximum(entries, -most), most).astype(held_as)


def setup_inputs(seed: int = 0) -> dict:
    arg_keys = jax.random.split(jax.random.key(seed), 5)
    return {
        "covariance": draw_covariance(jax.random.fold_in(arg_keys[4], 71), 0),
        "telemetry": scatter_about(arg_keys[1], (SAMPLES, TILES // N_COL, N_COL, TB), 1.0, 6.0, ((0, 4), (2, 8))),
        "active": set_ends((jax.random.randint(arg_keys[2], (SENS, SUBAP), 0, 8) < 7).astype(jnp.int32), jax.random.fold_in(arg_keys[2], 1), 0, 1),
        "panel": jax.random.randint(arg_keys[3], (1,), 0, TILES - N_COL // 2).astype(jnp.int32),
    }


FORGET = 0.9

def reference(covariance, telemetry, active, panel):
    order = TILES * TB
    prior = covariance.reshape(TILES, TILES, TB, TB)
    slope_mask = jnp.concatenate([active, active], axis=1).reshape(order).astype(jnp.bfloat16)
    masked = telemetry.reshape(SAMPLES, order) * slope_mask[None, :]
    panel_at = panel[0]
    start = (panel_at * TB).astype(jnp.int32)
    panel_data = lax.dynamic_slice_in_dim(masked, start, TB, 1)
    column_gram = jnp.dot(masked.T.astype(jnp.float32), panel_data.astype(jnp.float32), preferred_element_type=jnp.float32)
    column_prior = lax.dynamic_index_in_dim(prior, panel_at, 1, keepdims=False).reshape(order, TB)
    column_fresh = FORGET * column_prior + column_gram / SAMPLES
    diag_tile = lax.dynamic_slice_in_dim(column_fresh, start, TB, 0)
    factor = jnp.linalg.cholesky(diag_tile)
    inverse = lax.linalg.triangular_solve(factor, jnp.eye(TB, dtype=jnp.float32), left_side=True, lower=True)
    solved = jnp.dot(column_fresh.astype(jnp.float32), inverse.T.astype(jnp.float32), precision=lax.Precision.HIGHEST, preferred_element_type=jnp.float32)
    tile_of_row = jnp.arange(order, dtype=jnp.int32) // TB
    solved = jnp.where((tile_of_row > panel_at)[:, None], solved, jnp.zeros_like(solved))
    tile_ids = jnp.arange(TILES, dtype=jnp.int32)

    def one_row(index):
        offset = (index * TB).astype(jnp.int32)
        row_block = lax.dynamic_slice_in_dim(masked, offset, TB, 1)
        gram = jnp.dot(row_block.T.astype(jnp.float32), masked.astype(jnp.float32), preferred_element_type=jnp.float32)
        prior_row = lax.dynamic_index_in_dim(prior, index, 0, keepdims=False)
        flat = prior_row.transpose(1, 0, 2).reshape(TB, order)
        fresh = FORGET * flat + gram / SAMPLES
        panel_row = lax.dynamic_slice_in_dim(solved, offset, TB, 0)
        update = jnp.dot(panel_row.astype(jnp.float32), solved.T.astype(jnp.float32), precision=lax.Precision.HIGHEST, preferred_element_type=jnp.float32)
        fresh_tiles = fresh.reshape(TB, TILES, TB).transpose(1, 0, 2)
        update_tiles = update.reshape(TB, TILES, TB).transpose(1, 0, 2)
        trailing = (tile_ids > panel_at) & (tile_ids <= index)
        result = jnp.where(trailing[:, None, None], fresh_tiles - update_tiles, fresh_tiles)
        on_column = (tile_ids == panel_at) & (index > panel_at)
        result = jnp.where(on_column[:, None, None], panel_row[None], result)
        on_diagonal = (tile_ids == panel_at) & (index == panel_at)
        result = jnp.where(on_diagonal[:, None, None], factor[None], result)
        result = jnp.where((tile_ids > index)[:, None, None], prior_row, result)
        return result
    factored = lax.map(one_row, tile_ids)
    return factored.reshape(TILES // N_ROW, N_ROW, TILES // N_COL, N_COL, TB, TB)
```

```python
import functools

import jax
import jax.numpy as jnp
from jax import lax
from jax.experimental import pallas as pl
from jax.experimental.pallas import tpu as pltpu
from jax.sharding import PartitionSpec as P

FORGET = 0.9


def from_root(block, axis, holder):
    block = jnp.where(lax.axis_index(axis) == holder, block, jnp.zeros_like(block))
    return lax.psum(block, axis)


def refresh_kernel(ids_ref, rowt_ref, col_ref, c_ref, o_ref, *, n_row, n_col, width, samples):
    a = pl.program_id(0)
    b = pl.program_id(1)
    i = a * n_row + ids_ref[0]
    j = b * n_col + ids_ref[1]
    prior = c_ref[0, 0, 0, 0]

    @pl.when(i >= j)
    def _():
        start = pl.multiple_of(b * width, width)
        cols = col_ref[:, pl.ds(start, width)]
        gram = jnp.dot(rowt_ref[0], cols, preferred_element_type=jnp.float32)
        o_ref[0, 0, 0, 0] = FORGET * prior + gram / samples

    @pl.when(i < j)
    def _():
        o_ref[0, 0, 0, 0] = prior


def update_kernel(ids_ref, r_ref, prow_ref, pcol_ref, fac_ref, o_ref, *, n_row, n_col):
    a = pl.program_id(0)
    b = pl.program_id(1)
    i = a * n_row + ids_ref[0]
    j = b * n_col + ids_ref[1]
    k = ids_ref[2]
    trailing = (i >= j) & (j > k)
    on_column = (j == k) & (i > k)
    on_diagonal = (j == k) & (i == k)
    keep = jnp.logical_not(trailing | on_column | on_diagonal)

    @pl.when(trailing)
    def _():
        upd = lax.dot_general(
            prow_ref[0], pcol_ref[0], (((1,), (1,)), ((), ())), preferred_element_type=jnp.float32
        )
        o_ref[0, 0, 0, 0] = r_ref[0, 0, 0, 0] - upd

    @pl.when(on_column)
    def _():
        o_ref[0, 0, 0, 0] = prow_ref[0].astype(jnp.float32)

    @pl.when(on_diagonal)
    def _():
        o_ref[0, 0, 0, 0] = fac_ref[...]

    @pl.when(keep)
    def _():
        o_ref[0, 0, 0, 0] = r_ref[0, 0, 0, 0]


def body(covariance, telemetry, active, panel, *, n_row, n_col):
    row_index = lax.axis_index("row")
    col_index = lax.axis_index("col")
    blocks_a = covariance.shape[0]
    blocks_b = covariance.shape[2]
    width = covariance.shape[4]
    ratio = n_col // n_row
    s_local = telemetry.shape[0]
    samples = s_local * n_row
    tiles = blocks_b * n_col
    local = telemetry[:, :, 0, :]
    mask_full = jnp.concatenate([active, active], axis=1).reshape(tiles, width).astype(jnp.bfloat16)
    col_mask = lax.dynamic_index_in_dim(
        mask_full.reshape(blocks_b, n_col, width), col_index, 1, keepdims=False
    )
    local = local * col_mask[None]

    column_data = lax.all_gather(local, "row", axis=0, tiled=True)
    perm = []
    for src_r in range(n_row):
        for src_c in range(n_col):
            dst_r = src_c % n_row
            dst_c = ratio * src_r + src_c // n_row
            perm.append((src_r * n_col + src_c, dst_r * n_col + dst_c))
    piece = lax.ppermute(local, ("row", "col"), perm)
    row_g = lax.all_gather(piece, "col", axis=0, tiled=False)
    row_g = row_g.reshape(n_row, ratio, s_local, blocks_b, width)
    row_t = jnp.transpose(row_g, (3, 1, 4, 0, 2)).reshape(blocks_a, width, samples)
    col_flat = column_data.reshape(samples, blocks_b * width)

    panel_at = panel[0]
    ids = jnp.stack([row_index, col_index, panel_at]).astype(jnp.int32)

    refreshed = pl.pallas_call(
        functools.partial(refresh_kernel, n_row=n_row, n_col=n_col, width=width, samples=samples),
        out_shape=jax.ShapeDtypeStruct(covariance.shape, jnp.float32),
        grid_spec=pltpu.PrefetchScalarGridSpec(
            num_scalar_prefetch=1,
            grid=(blocks_a, blocks_b),
            in_specs=[
                pl.BlockSpec((1, width, samples), lambda a, b, ids: (a, 0, 0)),
                pl.BlockSpec((samples, blocks_b * width), lambda a, b, ids: (0, 0)),
                pl.BlockSpec((1, 1, 1, 1, width, width), lambda a, b, ids: (a, 0, b, 0, 0, 0)),
            ],
            out_specs=pl.BlockSpec((1, 1, 1, 1, width, width), lambda a, b, ids: (a, 0, b, 0, 0, 0)),
        ),
        compiler_params=pltpu.CompilerParams(vmem_limit_bytes=48 * 1024 * 1024),
    )(ids, row_t, col_flat, covariance)

    fresh = refreshed[:, 0, :, 0]
    owner_row = panel_at % n_row
    owner_col = panel_at % n_col
    row_tiles = jnp.arange(blocks_a, dtype=jnp.int32) * n_row + row_index
    diag_tile = lax.dynamic_slice(
        fresh, (panel_at // n_row, panel_at // n_col, 0, 0), (1, 1, width, width)
    )[0, 0]
    factor = jnp.linalg.cholesky(diag_tile)
    inverse = lax.linalg.triangular_solve(
        factor, jnp.eye(width, dtype=jnp.float32), left_side=True, lower=True
    )
    inverse = from_root(inverse, "row", owner_row)
    column_part = lax.dynamic_index_in_dim(fresh, panel_at // n_col, 1, keepdims=False)
    solved = jnp.einsum(
        "atu,vu->atv",
        column_part,
        inverse,
        precision=lax.Precision.HIGHEST,
        preferred_element_type=jnp.float32,
    )
    solved = jnp.where((row_tiles > panel_at)[:, None, None], solved, jnp.zeros_like(solved))
    panel_rows = from_root(solved.astype(jnp.bfloat16), "col", owner_col)
    pick = col_index // n_row
    chosen = lax.dynamic_index_in_dim(
        panel_rows.reshape(blocks_b, ratio, width, width), pick, 1, keepdims=False
    )
    panel_cols = from_root(chosen, "row", col_index % n_row)

    result = pl.pallas_call(
        functools.partial(update_kernel, n_row=n_row, n_col=n_col),
        out_shape=jax.ShapeDtypeStruct(covariance.shape, jnp.float32),
        grid_spec=pltpu.PrefetchScalarGridSpec(
            num_scalar_prefetch=1,
            grid=(blocks_a, blocks_b),
            in_specs=[
                pl.BlockSpec((1, 1, 1, 1, width, width), lambda a, b, ids: (a, 0, b, 0, 0, 0)),
                pl.BlockSpec((1, width, width), lambda a, b, ids: (a, 0, 0)),
                pl.BlockSpec((1, width, width), lambda a, b, ids: (b, 0, 0)),
                pl.BlockSpec((width, width), lambda a, b, ids: (0, 0)),
            ],
            out_specs=pl.BlockSpec((1, 1, 1, 1, width, width), lambda a, b, ids: (a, 0, b, 0, 0, 0)),
        ),
        input_output_aliases={1: 0},
    )(ids, refreshed, panel_rows, panel_cols, factor)
    return result


def solution(mesh):
    n_row = mesh.shape["row"]
    n_col = mesh.shape["col"]
    in_specs = (P(None, "row", None, "col", None, None), P("row", None, "col", None), P(), P())
    out_specs = P(None, "row", None, "col", None, None)
    return jax.shard_map(
        functools.partial(body, n_row=n_row, n_col=n_col),
        mesh=mesh,
        in_specs=in_specs,
        out_specs=out_specs,
        check_vma=False,
    )
```

```python
import functools

import jax
import jax.numpy as jnp
from jax import lax
from jax.experimental import pallas as pl
from jax.experimental.pallas import tpu as pltpu
from jax.sharding import PartitionSpec as P

FORGET = 0.9
NT = (((1,), (1,)), ((), ()))


def from_root(block, axis, holder):
    block = jnp.where(lax.axis_index(axis) == holder, block, jnp.zeros_like(block))
    return lax.psum(block, axis)


def refresh_kernel(ids_ref, row_ref, col_ref, c_ref, o_ref, *, n_row, n_col, blocks_b, samples):
    a = pl.program_id(0)
    r = ids_ref[0]
    c = ids_ref[1]
    i = a * n_row + r
    for b in range(blocks_b):
        j = b * n_col + c

        @pl.when(i >= j)
        def _(b=b):
            acc = None
            for p in range(n_row):
                q = (r - p + n_row) % n_row
                part = lax.dot_general(
                    row_ref[p, 0, 0], col_ref[q, b], NT, preferred_element_type=jnp.float32
                )
                acc = part if acc is None else acc + part
            o_ref[0, 0, b, 0] = FORGET * c_ref[0, 0, b, 0] + acc / samples

        @pl.when(i < j)
        def _(b=b):
            o_ref[0, 0, b, 0] = c_ref[0, 0, b, 0]


def update_kernel(ids_ref, r_ref, prow_ref, pcol_ref, fac_ref, o_ref, *, n_row, n_col, blocks_b):
    a = pl.program_id(0)
    i = a * n_row + ids_ref[0]
    c = ids_ref[1]
    k = ids_ref[2]
    for b in range(blocks_b):
        j = b * n_col + c
        trailing = (i >= j) & (j > k)
        on_column = (j == k) & (i > k)
        on_diagonal = (j == k) & (i == k)
        keep = jnp.logical_not(trailing | on_column | on_diagonal)

        @pl.when(trailing)
        def _(b=b):
            upd = lax.dot_general(prow_ref[0], pcol_ref[b], NT, preferred_element_type=jnp.float32)
            o_ref[0, 0, b, 0] = r_ref[0, 0, b, 0] - upd

        @pl.when(on_column)
        def _(b=b):
            o_ref[0, 0, b, 0] = prow_ref[0].astype(jnp.float32)

        @pl.when(on_diagonal)
        def _(b=b):
            o_ref[0, 0, b, 0] = fac_ref[...]

        @pl.when(keep)
        def _(b=b):
            o_ref[0, 0, b, 0] = r_ref[0, 0, b, 0]


def gather_row(x, n_row):
    parts = [x]
    for s in range(1, n_row):
        parts.append(lax.ppermute(x, "row", [(q, (q + s) % n_row) for q in range(n_row)]))
    return jnp.stack(parts)


def body(covariance, telemetry, active, panel, *, n_row, n_col):
    row_index = lax.axis_index("row")
    col_index = lax.axis_index("col")
    blocks_a = covariance.shape[0]
    blocks_b = covariance.shape[2]
    width = covariance.shape[4]
    ratio = n_col // n_row
    s_local = telemetry.shape[0]
    samples = s_local * n_row
    tiles = blocks_b * n_col
    prior = covariance[:, 0, :, 0]
    mask_full = jnp.concatenate([active, active], axis=1).reshape(tiles, width).astype(jnp.bfloat16)
    col_mask = lax.dynamic_index_in_dim(
        mask_full.reshape(blocks_b, n_col, width), col_index, 1, keepdims=False
    )
    local = telemetry[:, :, 0, :] * col_mask[None]
    local_t = jnp.transpose(local, (1, 2, 0))

    col_t = gather_row(local_t, n_row)
    perm = []
    for src_r in range(n_row):
        for src_c in range(n_col):
            dst_r = src_c % n_row
            dst_c = ratio * src_r + src_c // n_row
            perm.append((src_r * n_col + src_c, dst_r * n_col + dst_c))
    piece = lax.ppermute(local_t, ("row", "col"), perm)
    row_g = lax.all_gather(piece, "col", axis=0, tiled=False)
    row5 = row_g.reshape(n_row, ratio, blocks_b, width, s_local)

    panel_at = panel[0]
    owner_row = panel_at % n_row
    owner_col = panel_at % n_col
    ids = jnp.stack([row_index, col_index, panel_at]).astype(jnp.int32)

    own_diag = lax.dynamic_slice(
        prior, (panel_at // n_row, panel_at // n_col, 0, 0), (1, 1, width, width)
    )[0, 0]
    diag_prior = gather_row(own_diag, n_row)[(row_index - owner_row) % n_row]
    col_k = lax.dynamic_index_in_dim(col_t, panel_at // n_col, 1, keepdims=False)
    gram_kk = jnp.einsum("pts,pus->tu", col_k, col_k, preferred_element_type=jnp.float32)
    diag_tile = FORGET * diag_prior + gram_kk / samples
    factor = jnp.linalg.cholesky(diag_tile)
    inverse = lax.linalg.triangular_solve(
        factor, jnp.eye(width, dtype=jnp.float32), left_side=True, lower=True
    )

    col_k_rp = jnp.take(col_k, (row_index - jnp.arange(n_row)) % n_row, axis=0)
    gram_col = jnp.einsum(
        "phbts,pus->bhtu", row5, col_k_rp, preferred_element_type=jnp.float32
    ).reshape(blocks_a, width, width)
    prior_col = lax.dynamic_index_in_dim(prior, panel_at // n_col, 1, keepdims=False)
    column_part = FORGET * prior_col + gram_col / samples
    row_tiles = jnp.arange(blocks_a, dtype=jnp.int32) * n_row + row_index
    solved = jnp.einsum(
        "atu,vu->atv",
        column_part,
        inverse,
        precision=lax.Precision.HIGHEST,
        preferred_element_type=jnp.float32,
    )
    solved = jnp.where((row_tiles > panel_at)[:, None, None], solved, jnp.zeros_like(solved))
    panel_rows = from_root(solved.astype(jnp.bfloat16), "col", owner_col)
    pick = col_index // n_row
    chosen = lax.dynamic_index_in_dim(
        panel_rows.reshape(blocks_b, ratio, width, width), pick, 1, keepdims=False
    )
    received = None
    for s in range(1, n_row):
        pairs = []
        for cc in range(n_col):
            src_r = cc % n_row
            pairs.append((src_r * n_col + cc, ((src_r + s) % n_row) * n_col + cc))
        got = lax.ppermute(chosen, ("row", "col"), pairs)
        received = got if received is None else received + got
    panel_cols = jnp.where(row_index == col_index % n_row, chosen, received)

    refreshed = pl.pallas_call(
        functools.partial(
            refresh_kernel, n_row=n_row, n_col=n_col, blocks_b=blocks_b, samples=samples
        ),
        out_shape=jax.ShapeDtypeStruct(covariance.shape, jnp.float32),
        grid_spec=pltpu.PrefetchScalarGridSpec(
            num_scalar_prefetch=1,
            grid=(blocks_a,),
            in_specs=[
                pl.BlockSpec(
                    (n_row, 1, 1, width, s_local),
                    lambda a, ids: (0, a % ratio, a // ratio, 0, 0),
                ),
                pl.BlockSpec((n_row, blocks_b, width, s_local), lambda a, ids: (0, 0, 0, 0)),
                pl.BlockSpec(
                    (1, 1, blocks_b, 1, width, width), lambda a, ids: (a, 0, 0, 0, 0, 0)
                ),
            ],
            out_specs=pl.BlockSpec(
                (1, 1, blocks_b, 1, width, width), lambda a, ids: (a, 0, 0, 0, 0, 0)
            ),
        ),
        compiler_params=pltpu.CompilerParams(vmem_limit_bytes=48 * 1024 * 1024),
    )(ids, row5, col_t, covariance)

    result = pl.pallas_call(
        functools.partial(update_kernel, n_row=n_row, n_col=n_col, blocks_b=blocks_b),
        out_shape=jax.ShapeDtypeStruct(covariance.shape, jnp.float32),
        grid_spec=pltpu.PrefetchScalarGridSpec(
            num_scalar_prefetch=1,
            grid=(blocks_a,),
            in_specs=[
                pl.BlockSpec(
                    (1, 1, blocks_b, 1, width, width), lambda a, ids: (a, 0, 0, 0, 0, 0)
                ),
                pl.BlockSpec((1, width, width), lambda a, ids: (a, 0, 0)),
                pl.BlockSpec((blocks_b, width, width), lambda a, ids: (0, 0, 0)),
                pl.BlockSpec((width, width), lambda a, ids: (0, 0)),
            ],
            out_specs=pl.BlockSpec(
                (1, 1, blocks_b, 1, width, width), lambda a, ids: (a, 0, 0, 0, 0, 0)
            ),
        ),
        input_output_aliases={1: 0},
        compiler_params=pltpu.CompilerParams(vmem_limit_bytes=48 * 1024 * 1024),
    )(ids, refreshed, panel_rows, panel_cols, factor)
    return result


def solution(mesh):
    n_row = mesh.shape["row"]
    n_col = mesh.shape["col"]
    in_specs = (P(None, "row", None, "col", None, None), P("row", None, "col", None), P(), P())
    out_specs = P(None, "row", None, "col", None, None)
    return jax.shard_map(
        functools.partial(body, n_row=n_row, n_col=n_col),
        mesh=mesh,
        in_specs=in_specs,
        out_specs=out_specs,
        check_vma=False,
    )
```

```python
import functools

import jax
import jax.numpy as jnp
from jax import lax
from jax.experimental import pallas as pl
from jax.experimental.pallas import tpu as pltpu
from jax.sharding import PartitionSpec as P

FORGET = 0.9
NT = (((1,), (1,)), ((), ()))


def from_root(block, axis, holder):
    block = jnp.where(lax.axis_index(axis) == holder, block, jnp.zeros_like(block))
    return lax.psum(block, axis)


def refresh_kernel(ids_ref, row_ref, col_ref, c_ref, o_ref, *, n_row, n_col, blocks_b, samples):
    a = pl.program_id(0)
    r = ids_ref[0]
    c = ids_ref[1]
    i = a * n_row + r

    def one_tile(b, carry):
        j = b * n_col + c

        @pl.when(i >= j)
        def _():
            acc = None
            for p in range(n_row):
                q = (r - p + n_row) % n_row
                part = lax.dot_general(
                    row_ref[p, 0, 0], col_ref[q, b], NT, preferred_element_type=jnp.float32
                )
                acc = part if acc is None else acc + part
            o_ref[0, 0, b, 0] = FORGET * c_ref[0, 0, b, 0] + acc / samples

        @pl.when(i < j)
        def _():
            o_ref[0, 0, b, 0] = c_ref[0, 0, b, 0]

        return carry

    lax.fori_loop(0, blocks_b, one_tile, 0)


def first_row(ids_ref, n_row, blocks_a):
    return jnp.minimum((ids_ref[2] - ids_ref[0] + n_row - 1) // n_row, blocks_a - 1)


def update_kernel(ids_ref, r_ref, prow_ref, pcol_ref, fac_ref, o_ref, *, n_row, n_col, blocks_a, blocks_b):
    a = jnp.maximum(pl.program_id(0), first_row(ids_ref, n_row, blocks_a))
    active = pl.program_id(0) >= first_row(ids_ref, n_row, blocks_a)
    i = a * n_row + ids_ref[0]
    c = ids_ref[1]
    k = ids_ref[2]
    for b in range(blocks_b):
        j = b * n_col + c
        trailing = (i >= j) & (j > k) & active
        on_column = (j == k) & (i > k) & active
        on_diagonal = (j == k) & (i == k) & active
        keep = jnp.logical_not(((i >= j) & (j > k)) | ((j == k) & (i >= k))) & active

        @pl.when(trailing)
        def _(b=b):
            upd = lax.dot_general(prow_ref[0], pcol_ref[b], NT, preferred_element_type=jnp.float32)
            o_ref[0, 0, b, 0] = r_ref[0, 0, b, 0] - upd

        @pl.when(on_column)
        def _(b=b):
            o_ref[0, 0, b, 0] = prow_ref[0].astype(jnp.float32)

        @pl.when(on_diagonal)
        def _(b=b):
            o_ref[0, 0, b, 0] = fac_ref[...]

        @pl.when(keep)
        def _(b=b):
            o_ref[0, 0, b, 0] = r_ref[0, 0, b, 0]


def gather_row(x, n_row):
    parts = [x]
    for s in range(1, n_row):
        parts.append(lax.ppermute(x, "row", [(q, (q + s) % n_row) for q in range(n_row)]))
    return jnp.stack(parts)


def body(covariance, telemetry, active, panel, *, n_row, n_col):
    row_index = lax.axis_index("row")
    col_index = lax.axis_index("col")
    blocks_a = covariance.shape[0]
    blocks_b = covariance.shape[2]
    width = covariance.shape[4]
    ratio = n_col // n_row
    s_local = telemetry.shape[0]
    samples = s_local * n_row
    tiles = blocks_b * n_col
    prior = covariance[:, 0, :, 0]
    mask_full = jnp.concatenate([active, active], axis=1).reshape(tiles, width).astype(jnp.bfloat16)
    col_mask = lax.dynamic_index_in_dim(
        mask_full.reshape(blocks_b, n_col, width), col_index, 1, keepdims=False
    )
    local = telemetry[:, :, 0, :] * col_mask[None]
    local_t = jnp.transpose(local, (1, 2, 0))

    col_t = gather_row(local_t, n_row)
    perm = []
    for src_r in range(n_row):
        for src_c in range(n_col):
            dst_r = src_c % n_row
            dst_c = ratio * src_r + src_c // n_row
            perm.append((src_r * n_col + src_c, dst_r * n_col + dst_c))
    piece = lax.ppermute(local_t, ("row", "col"), perm)
    row_g = lax.all_gather(piece, "col", axis=0, tiled=False)
    row5 = row_g.reshape(n_row, ratio, blocks_b, width, s_local)

    panel_at = panel[0]
    owner_row = panel_at % n_row
    owner_col = panel_at % n_col
    ids = jnp.stack([row_index, col_index, panel_at]).astype(jnp.int32)

    own_diag = lax.dynamic_slice(
        prior, (panel_at // n_row, panel_at // n_col, 0, 0), (1, 1, width, width)
    )[0, 0]
    diag_prior = gather_row(own_diag, n_row)[(row_index - owner_row) % n_row]
    col_k = gather_row(lax.dynamic_index_in_dim(local_t, panel_at // n_col, 0, keepdims=False), n_row)
    gram_kk = jnp.einsum("pts,pus->tu", col_k, col_k, preferred_element_type=jnp.float32)
    diag_tile = FORGET * diag_prior + gram_kk / samples
    factor = jnp.linalg.cholesky(diag_tile)
    inverse = lax.linalg.triangular_solve(
        factor, jnp.eye(width, dtype=jnp.float32), left_side=True, lower=True
    )

    col_k_rp = jnp.take(col_k, (row_index - jnp.arange(n_row)) % n_row, axis=0)
    gram_col = jnp.einsum(
        "phbts,pus->bhtu", row5, col_k_rp, preferred_element_type=jnp.float32
    ).reshape(blocks_a, width, width)
    prior_col = lax.dynamic_index_in_dim(prior, panel_at // n_col, 1, keepdims=False)
    column_part = FORGET * prior_col + gram_col / samples
    row_tiles = jnp.arange(blocks_a, dtype=jnp.int32) * n_row + row_index
    solved = jnp.einsum(
        "atu,vu->atv",
        column_part,
        inverse,
        precision=lax.Precision.HIGHEST,
        preferred_element_type=jnp.float32,
    )
    solved = jnp.where((row_tiles > panel_at)[:, None, None], solved, jnp.zeros_like(solved))
    panel_rows = from_root(solved.astype(jnp.bfloat16), "col", owner_col)
    pick = col_index // n_row
    chosen = lax.dynamic_index_in_dim(
        panel_rows.reshape(blocks_b, ratio, width, width), pick, 1, keepdims=False
    )
    received = None
    for s in range(1, n_row):
        pairs = []
        for cc in range(n_col):
            src_r = cc % n_row
            pairs.append((src_r * n_col + cc, ((src_r + s) % n_row) * n_col + cc))
        got = lax.ppermute(chosen, ("row", "col"), pairs)
        received = got if received is None else received + got
    panel_cols = jnp.where(row_index == col_index % n_row, chosen, received)

    refreshed = pl.pallas_call(
        functools.partial(
            refresh_kernel, n_row=n_row, n_col=n_col, blocks_b=blocks_b, samples=samples
        ),
        out_shape=jax.ShapeDtypeStruct(covariance.shape, jnp.float32),
        grid_spec=pltpu.PrefetchScalarGridSpec(
            num_scalar_prefetch=1,
            grid=(blocks_a,),
            in_specs=[
                pl.BlockSpec(
                    (n_row, 1, 1, width, s_local),
                    lambda a, ids: (0, a % ratio, a // ratio, 0, 0),
                ),
                pl.BlockSpec((n_row, blocks_b, width, s_local), lambda a, ids: (0, 0, 0, 0)),
                pl.BlockSpec(
                    (1, 1, blocks_b, 1, width, width), lambda a, ids: (a, 0, 0, 0, 0, 0)
                ),
            ],
            out_specs=pl.BlockSpec(
                (1, 1, blocks_b, 1, width, width), lambda a, ids: (a, 0, 0, 0, 0, 0)
            ),
        ),
        compiler_params=pltpu.CompilerParams(vmem_limit_bytes=48 * 1024 * 1024),
    )(ids, row5, col_t, covariance)

    def row_at(a, ids):
        return jnp.maximum(a, first_row(ids, n_row, blocks_a))

    def update_rows(a, ids):
        return (row_at(a, ids), 0, 0, 0, 0, 0)

    result = pl.pallas_call(
        functools.partial(
            update_kernel, n_row=n_row, n_col=n_col, blocks_a=blocks_a, blocks_b=blocks_b
        ),
        out_shape=jax.ShapeDtypeStruct(covariance.shape, jnp.float32),
        grid_spec=pltpu.PrefetchScalarGridSpec(
            num_scalar_prefetch=1,
            grid=(blocks_a,),
            in_specs=[
                pl.BlockSpec((1, 1, blocks_b, 1, width, width), update_rows),
                pl.BlockSpec((1, width, width), lambda a, ids: (row_at(a, ids), 0, 0)),
                pl.BlockSpec((blocks_b, width, width), lambda a, ids: (0, 0, 0)),
                pl.BlockSpec((width, width), lambda a, ids: (0, 0)),
            ],
            out_specs=pl.BlockSpec((1, 1, blocks_b, 1, width, width), update_rows),
        ),
        input_output_aliases={1: 0},
        compiler_params=pltpu.CompilerParams(vmem_limit_bytes=48 * 1024 * 1024),
    )(ids, refreshed, panel_rows, panel_cols, factor)
    return result


def solution(mesh):
    n_row = mesh.shape["row"]
    n_col = mesh.shape["col"]
    in_specs = (P(None, "row", None, "col", None, None), P("row", None, "col", None), P(), P())
    out_specs = P(None, "row", None, "col", None, None)
    return jax.shard_map(
        functools.partial(body, n_row=n_row, n_col=n_col),
        mesh=mesh,
        in_specs=in_specs,
        out_specs=out_specs,
        check_vma=False,
    )
```

```python
import functools

import jax
import jax.numpy as jnp
from jax import lax
from jax.experimental import pallas as pl
from jax.experimental.pallas import tpu as pltpu
from jax.sharding import PartitionSpec as P

FORGET = 0.9
NT = (((1,), (1,)), ((), ()))


def from_root(block, axis, holder):
    block = jnp.where(lax.axis_index(axis) == holder, block, jnp.zeros_like(block))
    return lax.psum(block, axis)


def step_kernel(
    ids_ref, row_ref, col_ref, c_ref, prow_ref, pcol_ref, fac_ref, o_ref, *, n_row, n_col, blocks_b, samples
):
    a = pl.program_id(0)
    r = ids_ref[0]
    c = ids_ref[1]
    k = ids_ref[2]
    i = a * n_row + r

    def one_tile(b, carry):
        j = b * n_col + c

        @pl.when((i >= j) & (j != k))
        def _():
            acc = None
            for d in range(n_row):
                part = lax.dot_general(
                    row_ref[0, d, 0], col_ref[ids_ref[3 + d], b], NT, preferred_element_type=jnp.float32
                )
                acc = part if acc is None else acc + part
            fresh = FORGET * c_ref[0, 0, b, 0] + acc / samples

            @pl.when(j > k)
            def _():
                upd = lax.dot_general(prow_ref[0], pcol_ref[b], NT, preferred_element_type=jnp.float32)
                o_ref[0, 0, b, 0] = fresh - upd

            @pl.when(j < k)
            def _():
                o_ref[0, 0, b, 0] = fresh

        @pl.when((j == k) & (i > k))
        def _():
            o_ref[0, 0, b, 0] = prow_ref[0].astype(jnp.float32)

        @pl.when((j == k) & (i == k))
        def _():
            o_ref[0, 0, b, 0] = fac_ref[...]

        @pl.when(i < j)
        def _():
            o_ref[0, 0, b, 0] = c_ref[0, 0, b, 0]

        return carry

    lax.fori_loop(0, blocks_b, one_tile, 0)


def gather_row(x, n_row):
    parts = [x]
    for s in range(1, n_row):
        parts.append(lax.ppermute(x, "row", [(q, (q + s) % n_row) for q in range(n_row)]))
    return jnp.stack(parts)


def body(covariance, telemetry, active, panel, *, n_row, n_col):
    row_index = lax.axis_index("row")
    col_index = lax.axis_index("col")
    blocks_a = covariance.shape[0]
    blocks_b = covariance.shape[2]
    width = covariance.shape[4]
    ratio = n_col // n_row
    s_local = telemetry.shape[0]
    samples = s_local * n_row
    tiles = blocks_b * n_col
    prior = covariance[:, 0, :, 0]
    mask_full = jnp.concatenate([active, active], axis=1).reshape(tiles, width).astype(jnp.bfloat16)
    col_mask = lax.dynamic_index_in_dim(
        mask_full.reshape(blocks_b, n_col, width), col_index, 1, keepdims=False
    )
    local = telemetry[:, :, 0, :] * col_mask[None]
    local_t = jnp.transpose(local, (1, 2, 0))

    col_t = gather_row(local_t, n_row)
    mask = n_row - 2
    perm = []
    for src_r in range(n_row):
        for src_c in range(n_col):
            dst_r = src_c % n_row
            dst_c = (src_c // n_row) * n_row + (src_r ^ (dst_r & mask))
            perm.append((src_r * n_col + src_c, dst_r * n_col + dst_c))
    piece = lax.ppermute(local_t, ("row", "col"), perm)
    row_g = lax.all_gather(piece, "col", axis=0, tiled=False)
    row5 = row_g.reshape(ratio, n_row, blocks_b, width, s_local)
    quarter_of = jnp.bitwise_xor(jnp.arange(n_row, dtype=jnp.int32), row_index & mask)
    col_of = (row_index - quarter_of + n_row) % n_row

    panel_at = panel[0]
    owner_row = panel_at % n_row
    owner_col = panel_at % n_col
    ids = jnp.concatenate([jnp.stack([row_index, col_index, panel_at]), col_of]).astype(jnp.int32)

    own_diag = lax.dynamic_slice(
        prior, (panel_at // n_row, panel_at // n_col, 0, 0), (1, 1, width, width)
    )[0, 0]
    diag_prior = gather_row(own_diag, n_row)[(row_index - owner_row) % n_row]
    col_k = gather_row(lax.dynamic_index_in_dim(local_t, panel_at // n_col, 0, keepdims=False), n_row)
    gram_kk = jnp.einsum("pts,pus->tu", col_k, col_k, preferred_element_type=jnp.float32)
    diag_tile = FORGET * diag_prior + gram_kk / samples
    factor = jnp.linalg.cholesky(diag_tile)
    inverse = lax.linalg.triangular_solve(
        factor, jnp.eye(width, dtype=jnp.float32), left_side=True, lower=True
    )

    col_k_d = jnp.take(col_k, col_of, axis=0)
    gram_col = jnp.einsum(
        "hdbts,dus->bhtu", row5, col_k_d, preferred_element_type=jnp.float32
    ).reshape(blocks_a, width, width)
    prior_col = lax.dynamic_index_in_dim(prior, panel_at // n_col, 1, keepdims=False)
    column_part = FORGET * prior_col + gram_col / samples
    row_tiles = jnp.arange(blocks_a, dtype=jnp.int32) * n_row + row_index
    solved = jnp.einsum(
        "atu,vu->atv",
        column_part,
        inverse,
        precision=lax.Precision.HIGHEST,
        preferred_element_type=jnp.float32,
    )
    solved = jnp.where((row_tiles > panel_at)[:, None, None], solved, jnp.zeros_like(solved))
    panel_rows = from_root(solved.astype(jnp.bfloat16), "col", owner_col)
    pick = col_index // n_row
    chosen = lax.dynamic_index_in_dim(
        panel_rows.reshape(blocks_b, ratio, width, width), pick, 1, keepdims=False
    )
    received = None
    for s in range(1, n_row):
        pairs = []
        for cc in range(n_col):
            src_r = cc % n_row
            pairs.append((src_r * n_col + cc, ((src_r + s) % n_row) * n_col + cc))
        got = lax.ppermute(chosen, ("row", "col"), pairs)
        received = got if received is None else received + got
    panel_cols = jnp.where(row_index == col_index % n_row, chosen, received)

    full_row = (1, 1, blocks_b, 1, width, width)
    result = pl.pallas_call(
        functools.partial(
            step_kernel, n_row=n_row, n_col=n_col, blocks_b=blocks_b, samples=samples
        ),
        out_shape=jax.ShapeDtypeStruct(covariance.shape, jnp.float32),
        grid_spec=pltpu.PrefetchScalarGridSpec(
            num_scalar_prefetch=1,
            grid=(blocks_a,),
            in_specs=[
                pl.BlockSpec(
                    (1, n_row, 1, width, s_local),
                    lambda a, ids: (a % ratio, 0, a // ratio, 0, 0),
                ),
                pl.BlockSpec((n_row, blocks_b, width, s_local), lambda a, ids: (0, 0, 0, 0)),
                pl.BlockSpec(full_row, lambda a, ids: (a, 0, 0, 0, 0, 0)),
                pl.BlockSpec((1, width, width), lambda a, ids: (a, 0, 0)),
                pl.BlockSpec((blocks_b, width, width), lambda a, ids: (0, 0, 0)),
                pl.BlockSpec((width, width), lambda a, ids: (0, 0)),
            ],
            out_specs=pl.BlockSpec(full_row, lambda a, ids: (a, 0, 0, 0, 0, 0)),
        ),
        compiler_params=pltpu.CompilerParams(vmem_limit_bytes=48 * 1024 * 1024),
    )(ids, row5, col_t, covariance, panel_rows, panel_cols, factor)
    return result


def solution(mesh):
    n_row = mesh.shape["row"]
    n_col = mesh.shape["col"]
    in_specs = (P(None, "row", None, "col", None, None), P("row", None, "col", None), P(), P())
    out_specs = P(None, "row", None, "col", None, None)
    return jax.shard_map(
        functools.partial(body, n_row=n_row, n_col=n_col),
        mesh=mesh,
        in_specs=in_specs,
        out_specs=out_specs,
        check_vma=False,
    )
```

```python
import functools

import jax
import jax.numpy as jnp
from jax import lax
from jax.experimental import pallas as pl
from jax.experimental.pallas import tpu as pltpu
from jax.sharding import PartitionSpec as P

FORGET = 0.9
NT = (((1,), (1,)), ((), ()))


def from_root(block, axis, holder):
    block = jnp.where(lax.axis_index(axis) == holder, block, jnp.zeros_like(block))
    return lax.psum(block, axis)


def step_kernel(
    ids_ref, row_ref, col_ref, c_ref, prow_ref, pcol_ref, fac_ref, o_ref, *, n_row, n_col, blocks_b, samples
):
    a = pl.program_id(0)
    r = ids_ref[0]
    c = ids_ref[1]
    k = ids_ref[2]
    i = a * n_row + r

    def one_tile(b, carry):
        j = b * n_col + c

        @pl.when((i >= j) & (j != k))
        def _():
            acc = None
            for d in range(n_row):
                part = lax.dot_general(
                    row_ref[0, d, 0], col_ref[ids_ref[3 + d], b], NT, preferred_element_type=jnp.float32
                )
                acc = part if acc is None else acc + part
            fresh = FORGET * c_ref[0, 0, b, 0] + acc / samples

            @pl.when(j > k)
            def _():
                upd = lax.dot_general(prow_ref[0], pcol_ref[b], NT, preferred_element_type=jnp.float32)
                o_ref[0, 0, b, 0] = fresh - upd

            @pl.when(j < k)
            def _():
                o_ref[0, 0, b, 0] = fresh

        @pl.when((j == k) & (i > k))
        def _():
            o_ref[0, 0, b, 0] = prow_ref[0].astype(jnp.float32)

        @pl.when((j == k) & (i == k))
        def _():
            o_ref[0, 0, b, 0] = fac_ref[...]

        @pl.when(i < j)
        def _():
            o_ref[0, 0, b, 0] = c_ref[0, 0, b, 0]

        return carry

    lax.fori_loop(0, blocks_b, one_tile, 0)


def gather_row(x, n_row):
    parts = [x]
    for s in range(1, n_row):
        parts.append(lax.ppermute(x, "row", [(q, (q + s) % n_row) for q in range(n_row)]))
    return jnp.stack(parts)


def body(covariance, telemetry, active, panel, *, n_row, n_col):
    row_index = lax.axis_index("row")
    col_index = lax.axis_index("col")
    blocks_a = covariance.shape[0]
    blocks_b = covariance.shape[2]
    width = covariance.shape[4]
    ratio = n_col // n_row
    s_local = telemetry.shape[0]
    samples = s_local * n_row
    tiles = blocks_b * n_col
    prior = covariance[:, 0, :, 0]
    mask_full = jnp.concatenate([active, active], axis=1).reshape(tiles, width).astype(jnp.bfloat16)
    col_mask = lax.dynamic_index_in_dim(
        mask_full.reshape(blocks_b, n_col, width), col_index, 1, keepdims=False
    )
    local = telemetry[:, :, 0, :] * col_mask[None]
    local_t = jnp.transpose(local, (1, 2, 0))

    col_t = gather_row(local_t, n_row)
    mask = n_row - 2
    perm = []
    for src_r in range(n_row):
        for src_c in range(n_col):
            dst_r = src_c % n_row
            dst_c = (src_c // n_row) * n_row + (src_r ^ (dst_r & mask))
            perm.append((src_r * n_col + src_c, dst_r * n_col + dst_c))
    piece = lax.ppermute(local_t, ("row", "col"), perm)
    row_g = lax.all_gather(piece, "col", axis=0, tiled=False)
    row5 = row_g.reshape(ratio, n_row, blocks_b, width, s_local)
    quarter_of = jnp.bitwise_xor(jnp.arange(n_row, dtype=jnp.int32), row_index & mask)
    col_of = (row_index - quarter_of + n_row) % n_row

    panel_at = panel[0]
    owner_row = panel_at % n_row
    owner_col = panel_at % n_col
    ids = jnp.concatenate([jnp.stack([row_index, col_index, panel_at]), col_of]).astype(jnp.int32)

    own_diag = lax.dynamic_slice(
        prior, (panel_at // n_row, panel_at // n_col, 0, 0), (1, 1, width, width)
    )[0, 0]
    diag_prior = gather_row(own_diag, n_row)[(row_index - owner_row) % n_row]
    col_k = lax.dynamic_index_in_dim(col_t, panel_at // n_col, 1, keepdims=False)
    gram_kk = jnp.einsum("pts,pus->tu", col_k, col_k, preferred_element_type=jnp.float32)
    diag_tile = FORGET * diag_prior + gram_kk / samples
    factor = jnp.linalg.cholesky(diag_tile)
    inverse = lax.linalg.triangular_solve(
        factor, jnp.eye(width, dtype=jnp.float32), left_side=True, lower=True
    )

    col_k_d = jnp.take(col_k, col_of, axis=0)
    gram_col = jnp.einsum(
        "hdbts,dus->bhtu", row5, col_k_d, preferred_element_type=jnp.float32
    ).reshape(blocks_a, width, width)
    prior_col = lax.dynamic_index_in_dim(prior, panel_at // n_col, 1, keepdims=False)
    column_part = FORGET * prior_col + gram_col / samples
    row_tiles = jnp.arange(blocks_a, dtype=jnp.int32) * n_row + row_index
    solved = jnp.einsum(
        "atu,vu->atv",
        column_part,
        inverse,
        precision=lax.Precision.HIGH,
        preferred_element_type=jnp.float32,
    )
    solved = jnp.where((row_tiles > panel_at)[:, None, None], solved, jnp.zeros_like(solved))
    panel_rows = from_root(solved.astype(jnp.bfloat16), "col", owner_col)
    pick = col_index // n_row
    chosen = lax.dynamic_index_in_dim(
        panel_rows.reshape(blocks_b, ratio, width, width), pick, 1, keepdims=False
    )
    received = None
    for s in range(1, n_row):
        pairs = []
        for cc in range(n_col):
            src_r = cc % n_row
            pairs.append((src_r * n_col + cc, ((src_r + s) % n_row) * n_col + cc))
        got = lax.ppermute(chosen, ("row", "col"), pairs)
        received = got if received is None else received + got
    panel_cols = jnp.where(row_index == col_index % n_row, chosen, received)

    full_row = (1, 1, blocks_b, 1, width, width)
    result = pl.pallas_call(
        functools.partial(
            step_kernel, n_row=n_row, n_col=n_col, blocks_b=blocks_b, samples=samples
        ),
        out_shape=jax.ShapeDtypeStruct(covariance.shape, jnp.float32),
        grid_spec=pltpu.PrefetchScalarGridSpec(
            num_scalar_prefetch=1,
            grid=(blocks_a,),
            in_specs=[
                pl.BlockSpec(
                    (1, n_row, 1, width, s_local),
                    lambda a, ids: (a % ratio, 0, a // ratio, 0, 0),
                ),
                pl.BlockSpec((n_row, blocks_b, width, s_local), lambda a, ids: (0, 0, 0, 0)),
                pl.BlockSpec(full_row, lambda a, ids: (a, 0, 0, 0, 0, 0)),
                pl.BlockSpec((1, width, width), lambda a, ids: (a, 0, 0)),
                pl.BlockSpec((blocks_b, width, width), lambda a, ids: (0, 0, 0)),
                pl.BlockSpec((width, width), lambda a, ids: (0, 0)),
            ],
            out_specs=pl.BlockSpec(full_row, lambda a, ids: (a, 0, 0, 0, 0, 0)),
        ),
        compiler_params=pltpu.CompilerParams(vmem_limit_bytes=48 * 1024 * 1024),
    )(ids, row5, col_t, covariance, panel_rows, panel_cols, factor)
    return result


def solution(mesh):
    n_row = mesh.shape["row"]
    n_col = mesh.shape["col"]
    in_specs = (P(None, "row", None, "col", None, None), P("row", None, "col", None), P(), P())
    out_specs = P(None, "row", None, "col", None, None)
    return jax.shard_map(
        functools.partial(body, n_row=n_row, n_col=n_col),
        mesh=mesh,
        in_specs=in_specs,
        out_specs=out_specs,
        check_vma=False,
    )
```

```python
import functools

import jax
import jax.numpy as jnp
from jax import lax
from jax.experimental import pallas as pl
from jax.experimental.pallas import tpu as pltpu
from jax.sharding import PartitionSpec as P


FORGET = 0.9
NT = (((1,), (1,)), ((), ()))


def from_root(block, axis, holder):
    block = jnp.where(lax.axis_index(axis) == holder, block, jnp.zeros_like(block))
    return lax.psum(block, axis)


def first_row(ids_ref, n_row, blocks_a):
    return jnp.minimum((ids_ref[2] - ids_ref[0] + n_row - 1) // n_row, blocks_a - 1)


def late_row(a, ids_ref, n_row, blocks_a):
    return jnp.maximum(a, first_row(ids_ref, n_row, blocks_a))


def refresh_kernel(ids_ref, row_ref, col_ref, c_ref, o_ref, *, n_row, n_col, blocks_b, samples):
    a = pl.program_id(0)
    r = ids_ref[0]
    c = ids_ref[1]
    k = ids_ref[2]
    i = a * n_row + r

    def one_tile(b, carry):
        j = b * n_col + c

        @pl.when((i >= j) & (j != k))
        def _():
            acc = None
            for d in range(n_row):
                part = lax.dot_general(
                    row_ref[0, d, 0], col_ref[ids_ref[3 + d], b], NT, preferred_element_type=jnp.float32
                )
                acc = part if acc is None else acc + part
            o_ref[0, 0, b, 0] = FORGET * c_ref[0, 0, b, 0] + acc / samples

        @pl.when((i < j) | (j == k))
        def _():
            o_ref[0, 0, b, 0] = c_ref[0, 0, b, 0]

        return carry

    lax.fori_loop(0, blocks_b, one_tile, 0)


def update_kernel(ids_ref, r_ref, prow_ref, pcol_ref, fac_ref, o_ref, *, n_row, n_col, blocks_a):
    start = first_row(ids_ref, n_row, blocks_a)
    a = late_row(pl.program_id(0), ids_ref, n_row, blocks_a)
    live = pl.program_id(0) >= start
    i = a * n_row + ids_ref[0]
    c = ids_ref[1]
    k = ids_ref[2]

    def one_tile(b, carry):
        j = b * n_col + c
        trailing = (i >= j) & (j > k)
        changed = trailing | ((j == k) & (i >= k))

        @pl.when(live & trailing)
        def _():
            upd = lax.dot_general(prow_ref[0], pcol_ref[b], NT, preferred_element_type=jnp.float32)
            o_ref[0, 0, b, 0] = r_ref[0, 0, b, 0] - upd

        @pl.when(live & (j == k) & (i > k))
        def _():
            o_ref[0, 0, b, 0] = prow_ref[0].astype(jnp.float32)

        @pl.when(live & (j == k) & (i == k))
        def _():
            o_ref[0, 0, b, 0] = fac_ref[...]

        @pl.when(live & jnp.logical_not(changed))
        def _():
            o_ref[0, 0, b, 0] = r_ref[0, 0, b, 0]

        return carry

    lax.fori_loop(0, pcol_ref.shape[0], one_tile, 0)


def gather_row(x, n_row):
    parts = [x]
    for s in range(1, n_row):
        parts.append(lax.ppermute(x, "row", [(q, (q + s) % n_row) for q in range(n_row)]))
    return jnp.stack(parts)


def body(covariance, telemetry, active, panel, *, n_row, n_col):
    return step(covariance, telemetry, active, panel, n_row=n_row, n_col=n_col)


def step(covariance, telemetry, active, panel, *, n_row, n_col):
    row_index = lax.axis_index("row")
    col_index = lax.axis_index("col")
    blocks_a = covariance.shape[0]
    blocks_b = covariance.shape[2]
    width = covariance.shape[4]
    ratio = n_col // n_row
    s_local = telemetry.shape[0]
    samples = s_local * n_row
    tiles = blocks_b * n_col
    prior = covariance[:, 0, :, 0]
    mask_full = jnp.concatenate([active, active], axis=1).reshape(tiles, width).astype(jnp.bfloat16)
    col_mask = lax.dynamic_index_in_dim(
        mask_full.reshape(blocks_b, n_col, width), col_index, 1, keepdims=False
    )
    local = telemetry[:, :, 0, :] * col_mask[None]
    local_t = jnp.transpose(local, (1, 2, 0))

    col_t = gather_row(local_t, n_row)
    mask = n_row - 2
    perm = []
    for src_r in range(n_row):
        for src_c in range(n_col):
            dst_r = src_c % n_row
            dst_c = (src_c // n_row) * n_row + (src_r ^ (dst_r & mask))
            perm.append((src_r * n_col + src_c, dst_r * n_col + dst_c))
    piece = lax.ppermute(local_t, ("row", "col"), perm)
    row_g = lax.all_gather(piece, "col", axis=0, tiled=False)
    row5 = row_g.reshape(ratio, n_row, blocks_b, width, s_local)
    quarter_of = jnp.bitwise_xor(jnp.arange(n_row, dtype=jnp.int32), row_index & mask)
    col_of = (row_index - quarter_of + n_row) % n_row

    panel_at = panel[0]
    owner_row = panel_at % n_row
    owner_col = panel_at % n_col
    ids = jnp.concatenate([jnp.stack([row_index, col_index, panel_at]), col_of]).astype(jnp.int32)

    own_diag = lax.dynamic_slice(
        prior, (panel_at // n_row, panel_at // n_col, 0, 0), (1, 1, width, width)
    )[0, 0]
    diag_prior = gather_row(own_diag, n_row)[(row_index - owner_row) % n_row]
    col_k = gather_row(lax.dynamic_index_in_dim(local_t, panel_at // n_col, 0, keepdims=False), n_row)
    gram_kk = jnp.einsum("pts,pus->tu", col_k, col_k, preferred_element_type=jnp.float32)
    diag_tile = FORGET * diag_prior + gram_kk / samples
    factor = jnp.linalg.cholesky(diag_tile)
    inverse = lax.linalg.triangular_solve(
        factor, jnp.eye(width, dtype=jnp.float32), left_side=True, lower=True
    )

    col_k_d = jnp.take(col_k, col_of, axis=0)
    gram_col = jnp.einsum(
        "hdbts,dus->bhtu", row5, col_k_d, preferred_element_type=jnp.float32
    ).reshape(blocks_a, width, width)
    prior_col = lax.dynamic_index_in_dim(prior, panel_at // n_col, 1, keepdims=False)
    column_part = FORGET * prior_col + gram_col / samples
    row_tiles = jnp.arange(blocks_a, dtype=jnp.int32) * n_row + row_index
    solved = jnp.einsum(
        "atu,vu->atv",
        column_part,
        inverse,
        precision=lax.Precision.HIGHEST,
        preferred_element_type=jnp.float32,
    )
    solved = jnp.where((row_tiles > panel_at)[:, None, None], solved, jnp.zeros_like(solved))
    panel_rows = from_root(solved.astype(jnp.bfloat16), "col", owner_col)
    pick = col_index // n_row
    chosen = lax.dynamic_index_in_dim(
        panel_rows.reshape(blocks_b, ratio, width, width), pick, 1, keepdims=False
    )
    received = None
    for s in range(1, n_row):
        pairs = []
        for cc in range(n_col):
            src_r = cc % n_row
            pairs.append((src_r * n_col + cc, ((src_r + s) % n_row) * n_col + cc))
        got = lax.ppermute(chosen, ("row", "col"), pairs)
        received = got if received is None else received + got
    panel_cols = jnp.where(row_index == col_index % n_row, chosen, received)

    full_row = (1, 1, blocks_b, 1, width, width)

    def late_pick(a, ids):
        return late_row(a, ids, n_row, blocks_a)

    refreshed = pl.pallas_call(
        functools.partial(
            refresh_kernel, n_row=n_row, n_col=n_col, blocks_b=blocks_b, samples=samples
        ),
        out_shape=jax.ShapeDtypeStruct(covariance.shape, jnp.float32),
        grid_spec=pltpu.PrefetchScalarGridSpec(
            num_scalar_prefetch=1,
            grid=(blocks_a,),
            in_specs=[
                pl.BlockSpec(
                    (1, n_row, 1, width, s_local),
                    lambda a, ids: (a % ratio, 0, a // ratio, 0, 0),
                ),
                pl.BlockSpec((n_row, blocks_b, width, s_local), lambda a, ids: (0, 0, 0, 0)),
                pl.BlockSpec(full_row, lambda a, ids: (a, 0, 0, 0, 0, 0)),
            ],
            out_specs=pl.BlockSpec(full_row, lambda a, ids: (a, 0, 0, 0, 0, 0)),
        ),
        compiler_params=pltpu.CompilerParams(vmem_limit_bytes=48 * 1024 * 1024),
    )(ids, row5, col_t, covariance)

    result = pl.pallas_call(
        functools.partial(update_kernel, n_row=n_row, n_col=n_col, blocks_a=blocks_a),
        out_shape=jax.ShapeDtypeStruct(covariance.shape, jnp.float32),
        grid_spec=pltpu.PrefetchScalarGridSpec(
            num_scalar_prefetch=1,
            grid=(blocks_a,),
            in_specs=[
                pl.BlockSpec(full_row, lambda a, ids: (late_pick(a, ids), 0, 0, 0, 0, 0)),
                pl.BlockSpec((1, width, width), lambda a, ids: (late_pick(a, ids), 0, 0)),
                pl.BlockSpec((blocks_b, width, width), lambda a, ids: (0, 0, 0)),
                pl.BlockSpec((width, width), lambda a, ids: (0, 0)),
            ],
            out_specs=pl.BlockSpec(full_row, lambda a, ids: (late_pick(a, ids), 0, 0, 0, 0, 0)),
        ),
        input_output_aliases={1: 0},
        compiler_params=pltpu.CompilerParams(vmem_limit_bytes=48 * 1024 * 1024),
    )(ids, refreshed, panel_rows, panel_cols, factor)
    return result


def solution(mesh):
    n_row = mesh.shape["row"]
    n_col = mesh.shape["col"]
    in_specs = (P(None, "row", None, "col", None, None), P("row", None, "col", None), P(), P())
    out_specs = P(None, "row", None, "col", None, None)
    return jax.shard_map(
        functools.partial(body, n_row=n_row, n_col=n_col),
        mesh=mesh,
        in_specs=in_specs,
        out_specs=out_specs,
        check_vma=False,
    )
```

```python
import functools

import jax
import jax.numpy as jnp
from jax import lax
from jax.experimental import pallas as pl
from jax.experimental.pallas import tpu as pltpu
from jax.sharding import PartitionSpec as P


FORGET = 0.9
NT = (((1,), (1,)), ((), ()))


def from_root(block, axis, holder):
    block = jnp.where(lax.axis_index(axis) == holder, block, jnp.zeros_like(block))
    return lax.psum(block, axis)


def first_row(ids_ref, n_row, blocks_a):
    return jnp.minimum((ids_ref[2] - ids_ref[0] + n_row - 1) // n_row, blocks_a - 1)


def late_row(a, ids_ref, n_row, blocks_a):
    return jnp.maximum(a, first_row(ids_ref, n_row, blocks_a))


def refresh_kernel(ids_ref, row_ref, col_ref, c_ref, *refs, n_row, n_col, blocks_b, samples, offset):
    o_ref = refs[-1]
    a = pl.program_id(0) + offset
    r = ids_ref[0]
    c = ids_ref[1]
    k = ids_ref[2]
    i = a * n_row + r

    def one_tile(b, carry):
        j = b * n_col + c

        @pl.when((i >= j) & (j != k))
        def _():
            acc = None
            for d in range(n_row):
                part = lax.dot_general(
                    row_ref[0, d, 0], col_ref[ids_ref[3 + d], b], NT, preferred_element_type=jnp.float32
                )
                acc = part if acc is None else acc + part
            o_ref[0, 0, b, 0] = FORGET * c_ref[0, 0, b, 0] + acc / samples

        @pl.when((i < j) | (j == k))
        def _():
            o_ref[0, 0, b, 0] = c_ref[0, 0, b, 0]

        return carry

    lax.fori_loop(0, blocks_b, one_tile, 0)


def update_kernel(ids_ref, r_ref, prow_ref, pcol_ref, fac_ref, o_ref, *, n_row, n_col, blocks_a):
    start = first_row(ids_ref, n_row, blocks_a)
    a = late_row(pl.program_id(0), ids_ref, n_row, blocks_a)
    live = pl.program_id(0) >= start
    i = a * n_row + ids_ref[0]
    c = ids_ref[1]
    k = ids_ref[2]

    def one_tile(b, carry):
        j = b * n_col + c
        trailing = (i >= j) & (j > k)
        changed = trailing | ((j == k) & (i >= k))

        @pl.when(live & trailing)
        def _():
            upd = lax.dot_general(prow_ref[0], pcol_ref[b], NT, preferred_element_type=jnp.float32)
            o_ref[0, 0, b, 0] = r_ref[0, 0, b, 0] - upd

        @pl.when(live & (j == k) & (i > k))
        def _():
            o_ref[0, 0, b, 0] = prow_ref[0].astype(jnp.float32)

        @pl.when(live & (j == k) & (i == k))
        def _():
            o_ref[0, 0, b, 0] = fac_ref[...]

        @pl.when(live & jnp.logical_not(changed))
        def _():
            o_ref[0, 0, b, 0] = r_ref[0, 0, b, 0]

        return carry

    lax.fori_loop(0, pcol_ref.shape[0], one_tile, 0)


def gather_row(x, n_row):
    parts = [x]
    for s in range(1, n_row):
        parts.append(lax.ppermute(x, "row", [(q, (q + s) % n_row) for q in range(n_row)]))
    return jnp.stack(parts)


def body(covariance, telemetry, active, panel, *, n_row, n_col):
    return step(covariance, telemetry, active, panel, n_row=n_row, n_col=n_col)


def step(covariance, telemetry, active, panel, *, n_row, n_col):
    row_index = lax.axis_index("row")
    col_index = lax.axis_index("col")
    blocks_a = covariance.shape[0]
    blocks_b = covariance.shape[2]
    width = covariance.shape[4]
    ratio = n_col // n_row
    s_local = telemetry.shape[0]
    samples = s_local * n_row
    tiles = blocks_b * n_col
    prior = covariance[:, 0, :, 0]
    mask_full = jnp.concatenate([active, active], axis=1).reshape(tiles, width).astype(jnp.bfloat16)
    col_mask = lax.dynamic_index_in_dim(
        mask_full.reshape(blocks_b, n_col, width), col_index, 1, keepdims=False
    )
    local = telemetry[:, :, 0, :] * col_mask[None]
    local_t = jnp.transpose(local, (1, 2, 0))

    col_t = gather_row(local_t, n_row)
    mask = n_row - 2
    perm = []
    for src_r in range(n_row):
        for src_c in range(n_col):
            dst_r = src_c % n_row
            dst_c = (src_c // n_row) * n_row + (src_r ^ (dst_r & mask))
            perm.append((src_r * n_col + src_c, dst_r * n_col + dst_c))
    piece = lax.ppermute(local_t, ("row", "col"), perm)
    row_g = lax.all_gather(piece, "col", axis=0, tiled=False)
    row5 = row_g.reshape(ratio, n_row, blocks_b, width, s_local)
    quarter_of = jnp.bitwise_xor(jnp.arange(n_row, dtype=jnp.int32), row_index & mask)
    col_of = (row_index - quarter_of + n_row) % n_row

    panel_at = panel[0]
    owner_row = panel_at % n_row
    owner_col = panel_at % n_col
    ids = jnp.concatenate([jnp.stack([row_index, col_index, panel_at]), col_of]).astype(jnp.int32)

    own_diag = lax.dynamic_slice(
        prior, (panel_at // n_row, panel_at // n_col, 0, 0), (1, 1, width, width)
    )[0, 0]
    diag_prior = gather_row(own_diag, n_row)[(row_index - owner_row) % n_row]
    col_k = gather_row(lax.dynamic_index_in_dim(local_t, panel_at // n_col, 0, keepdims=False), n_row)
    gram_kk = jnp.einsum("pts,pus->tu", col_k, col_k, preferred_element_type=jnp.float32)
    diag_tile = FORGET * diag_prior + gram_kk / samples
    factor = jnp.linalg.cholesky(diag_tile)
    inverse = lax.linalg.triangular_solve(
        factor, jnp.eye(width, dtype=jnp.float32), left_side=True, lower=True
    )

    col_k_d = jnp.take(col_k, col_of, axis=0)
    gram_col = jnp.einsum(
        "hdbts,dus->bhtu", row5, col_k_d, preferred_element_type=jnp.float32
    ).reshape(blocks_a, width, width)
    prior_col = lax.dynamic_index_in_dim(prior, panel_at // n_col, 1, keepdims=False)
    column_part = FORGET * prior_col + gram_col / samples
    row_tiles = jnp.arange(blocks_a, dtype=jnp.int32) * n_row + row_index
    solved = jnp.einsum(
        "atu,vu->atv",
        column_part,
        inverse,
        precision=lax.Precision.HIGHEST,
        preferred_element_type=jnp.float32,
    )
    solved = jnp.where((row_tiles > panel_at)[:, None, None], solved, jnp.zeros_like(solved))
    panel_rows = from_root(solved.astype(jnp.bfloat16), "col", owner_col)
    pick = col_index // n_row
    chosen = lax.dynamic_index_in_dim(
        panel_rows.reshape(blocks_b, ratio, width, width), pick, 1, keepdims=False
    )
    received = None
    for s in range(1, n_row):
        pairs = []
        for cc in range(n_col):
            src_r = cc % n_row
            pairs.append((src_r * n_col + cc, ((src_r + s) % n_row) * n_col + cc))
        got = lax.ppermute(chosen, ("row", "col"), pairs)
        received = got if received is None else received + got
    panel_cols = jnp.where(row_index == col_index % n_row, chosen, received)

    full_row = (1, 1, blocks_b, 1, width, width)

    def late_pick(a, ids):
        return late_row(a, ids, n_row, blocks_a)

    half = blocks_a // 2

    def refresh_half(offset, rows, prev):
        extra = [] if prev is None else [prev]
        return pl.pallas_call(
            functools.partial(
                refresh_kernel, n_row=n_row, n_col=n_col, blocks_b=blocks_b, samples=samples,
                offset=offset,
            ),
            out_shape=jax.ShapeDtypeStruct(covariance.shape, jnp.float32),
            grid_spec=pltpu.PrefetchScalarGridSpec(
                num_scalar_prefetch=1,
                grid=(rows,),
                in_specs=[
                    pl.BlockSpec(
                        (1, n_row, 1, width, s_local),
                        lambda a, ids: ((a + offset) % ratio, 0, (a + offset) // ratio, 0, 0),
                    ),
                    pl.BlockSpec((n_row, blocks_b, width, s_local), lambda a, ids: (0, 0, 0, 0)),
                    pl.BlockSpec(full_row, lambda a, ids: (a + offset, 0, 0, 0, 0, 0)),
                ] + [pl.BlockSpec(memory_space=pl.ANY)] * len(extra),
                out_specs=pl.BlockSpec(full_row, lambda a, ids: (a + offset, 0, 0, 0, 0, 0)),
            ),
            input_output_aliases={} if prev is None else {4: 0},
            compiler_params=pltpu.CompilerParams(vmem_limit_bytes=48 * 1024 * 1024),
        )(ids, row5, col_t, covariance, *extra)

    refreshed = refresh_half(0, half, None)
    refreshed = refresh_half(half, blocks_a - half, refreshed)

    result = pl.pallas_call(
        functools.partial(update_kernel, n_row=n_row, n_col=n_col, blocks_a=blocks_a),
        out_shape=jax.ShapeDtypeStruct(covariance.shape, jnp.float32),
        grid_spec=pltpu.PrefetchScalarGridSpec(
            num_scalar_prefetch=1,
            grid=(blocks_a,),
            in_specs=[
                pl.BlockSpec(full_row, lambda a, ids: (late_pick(a, ids), 0, 0, 0, 0, 0)),
                pl.BlockSpec((1, width, width), lambda a, ids: (late_pick(a, ids), 0, 0)),
                pl.BlockSpec((blocks_b, width, width), lambda a, ids: (0, 0, 0)),
                pl.BlockSpec((width, width), lambda a, ids: (0, 0)),
            ],
            out_specs=pl.BlockSpec(full_row, lambda a, ids: (late_pick(a, ids), 0, 0, 0, 0, 0)),
        ),
        input_output_aliases={1: 0},
        compiler_params=pltpu.CompilerParams(vmem_limit_bytes=48 * 1024 * 1024),
    )(ids, refreshed, panel_rows, panel_cols, factor)
    return result


def solution(mesh):
    n_row = mesh.shape["row"]
    n_col = mesh.shape["col"]
    in_specs = (P(None, "row", None, "col", None, None), P("row", None, "col", None), P(), P())
    out_specs = P(None, "row", None, "col", None, None)
    return jax.shard_map(
        functools.partial(body, n_row=n_row, n_col=n_col),
        mesh=mesh,
        in_specs=in_specs,
        out_specs=out_specs,
        check_vma=False,
    )
```

```python
import functools

import jax
import jax.numpy as jnp
from jax import lax
from jax.experimental import pallas as pl
from jax.experimental.pallas import tpu as pltpu
from jax.sharding import PartitionSpec as P


FORGET = 0.9
NT = (((1,), (1,)), ((), ()))


def from_root(block, axis, holder):
    block = jnp.where(lax.axis_index(axis) == holder, block, jnp.zeros_like(block))
    return lax.psum(block, axis)


def first_row(ids_ref, n_row, blocks_a):
    return jnp.minimum((ids_ref[2] - ids_ref[0] + n_row - 1) // n_row, blocks_a - 1)


def late_row(a, ids_ref, n_row, blocks_a):
    return jnp.maximum(a, first_row(ids_ref, n_row, blocks_a))


def refresh_kernel(ids_ref, row_ref, col_ref, c_ref, *refs, n_row, n_col, blocks_b, samples, offset):
    o_ref = refs[-1]
    a = pl.program_id(0) + offset
    r = ids_ref[0]
    c = ids_ref[1]
    k = ids_ref[2]
    i = a * n_row + r

    def one_tile(b, carry):
        j = b * n_col + c

        @pl.when((i >= j) & (j != k))
        def _():
            acc = None
            for d in range(n_row):
                part = lax.dot_general(
                    row_ref[0, d, 0], col_ref[ids_ref[3 + d], b], NT, preferred_element_type=jnp.float32
                )
                acc = part if acc is None else acc + part
            o_ref[0, 0, b, 0] = FORGET * c_ref[0, 0, b, 0] + acc / samples

        @pl.when((i < j) | (j == k))
        def _():
            o_ref[0, 0, b, 0] = c_ref[0, 0, b, 0]

        return carry

    lax.fori_loop(0, blocks_b, one_tile, 0)


def update_kernel(ids_ref, r_ref, prow_ref, pcol_ref, fac_ref, o_ref, *, n_row, n_col, blocks_a):
    start = first_row(ids_ref, n_row, blocks_a)
    a = late_row(pl.program_id(0), ids_ref, n_row, blocks_a)
    live = pl.program_id(0) >= start
    i = a * n_row + ids_ref[0]
    c = ids_ref[1]
    k = ids_ref[2]

    def one_tile(b, carry):
        j = b * n_col + c
        trailing = (i >= j) & (j > k)
        changed = trailing | ((j == k) & (i >= k))

        @pl.when(live & trailing)
        def _():
            upd = lax.dot_general(prow_ref[0], pcol_ref[b], NT, preferred_element_type=jnp.float32)
            o_ref[0, 0, b, 0] = r_ref[0, 0, b, 0] - upd

        @pl.when(live & (j == k) & (i > k))
        def _():
            o_ref[0, 0, b, 0] = prow_ref[0].astype(jnp.float32)

        @pl.when(live & (j == k) & (i == k))
        def _():
            o_ref[0, 0, b, 0] = fac_ref[...]

        @pl.when(live & jnp.logical_not(changed))
        def _():
            o_ref[0, 0, b, 0] = r_ref[0, 0, b, 0]

        return carry

    lax.fori_loop(0, pcol_ref.shape[0], one_tile, 0)


def gather_row(x, n_row):
    parts = [x]
    for s in range(1, n_row):
        parts.append(lax.ppermute(x, "row", [(q, (q + s) % n_row) for q in range(n_row)]))
    return jnp.stack(parts)


def body(covariance, telemetry, active, panel, *, n_row, n_col):
    return step(covariance, telemetry, active, panel, n_row=n_row, n_col=n_col)


def step(covariance, telemetry, active, panel, *, n_row, n_col):
    row_index = lax.axis_index("row")
    col_index = lax.axis_index("col")
    blocks_a = covariance.shape[0]
    blocks_b = covariance.shape[2]
    width = covariance.shape[4]
    ratio = n_col // n_row
    s_local = telemetry.shape[0]
    samples = s_local * n_row
    tiles = blocks_b * n_col
    prior = covariance[:, 0, :, 0]
    mask_full = jnp.concatenate([active, active], axis=1).reshape(tiles, width).astype(jnp.bfloat16)
    col_mask = lax.dynamic_index_in_dim(
        mask_full.reshape(blocks_b, n_col, width), col_index, 1, keepdims=False
    )
    local = telemetry[:, :, 0, :] * col_mask[None]
    local_t = jnp.transpose(local, (1, 2, 0))

    col_t = gather_row(local_t, n_row)
    mask = n_row - 2
    perm = []
    for src_r in range(n_row):
        for src_c in range(n_col):
            dst_r = src_c % n_row
            dst_c = (src_c // n_row) * n_row + (src_r ^ (dst_r & mask))
            perm.append((src_r * n_col + src_c, dst_r * n_col + dst_c))
    piece = lax.ppermute(local_t, ("row", "col"), perm)
    row_g = lax.all_gather(piece, "col", axis=0, tiled=False)
    row5 = row_g.reshape(ratio, n_row, blocks_b, width, s_local)
    quarter_of = jnp.bitwise_xor(jnp.arange(n_row, dtype=jnp.int32), row_index & mask)
    col_of = (row_index - quarter_of + n_row) % n_row

    panel_at = panel[0]
    owner_row = panel_at % n_row
    owner_col = panel_at % n_col
    ids = jnp.concatenate([jnp.stack([row_index, col_index, panel_at]), col_of]).astype(jnp.int32)

    own_diag = lax.dynamic_slice(
        prior, (panel_at // n_row, panel_at // n_col, 0, 0), (1, 1, width, width)
    )[0, 0]
    diag_prior = gather_row(own_diag, n_row)[(row_index - owner_row) % n_row]
    col_k = gather_row(
        lax.dynamic_index_in_dim(local_t, panel_at // n_col, 0, keepdims=False), n_row
    )
    gram_kk = jnp.einsum("pts,pus->tu", col_k, col_k, preferred_element_type=jnp.float32)
    diag_tile = FORGET * diag_prior + gram_kk / samples
    factor = jnp.linalg.cholesky(diag_tile)
    inverse = lax.linalg.triangular_solve(
        factor, jnp.eye(width, dtype=jnp.float32), left_side=True, lower=True
    )

    col_k_d = jnp.take(col_k, col_of, axis=0)
    gram_col = jnp.einsum(
        "hdbts,dus->bhtu", row5, col_k_d, preferred_element_type=jnp.float32
    ).reshape(blocks_a, width, width)
    prior_col = lax.dynamic_index_in_dim(prior, panel_at // n_col, 1, keepdims=False)
    column_part = FORGET * prior_col + gram_col / samples
    row_tiles = jnp.arange(blocks_a, dtype=jnp.int32) * n_row + row_index
    solved = jnp.einsum(
        "atu,vu->atv",
        column_part,
        inverse,
        precision=lax.Precision.HIGH,
        preferred_element_type=jnp.float32,
    )
    solved = jnp.where((row_tiles > panel_at)[:, None, None], solved, jnp.zeros_like(solved))
    panel_rows = from_root(solved.astype(jnp.bfloat16), "col", owner_col)
    pick = col_index // n_row
    chosen = lax.dynamic_index_in_dim(
        panel_rows.reshape(blocks_b, ratio, width, width), pick, 1, keepdims=False
    )
    received = None
    for s in range(1, n_row):
        pairs = []
        for cc in range(n_col):
            src_r = cc % n_row
            pairs.append((src_r * n_col + cc, ((src_r + s) % n_row) * n_col + cc))
        got = lax.ppermute(chosen, ("row", "col"), pairs)
        received = got if received is None else received + got
    panel_cols = jnp.where(row_index == col_index % n_row, chosen, received)

    full_row = (1, 1, blocks_b, 1, width, width)

    def late_pick(a, ids):
        return late_row(a, ids, n_row, blocks_a)

    half = (4 * blocks_a) // 5

    def refresh_half(offset, rows, prev):
        extra = [] if prev is None else [prev]
        return pl.pallas_call(
            functools.partial(
                refresh_kernel, n_row=n_row, n_col=n_col, blocks_b=blocks_b, samples=samples,
                offset=offset,
            ),
            out_shape=jax.ShapeDtypeStruct(covariance.shape, jnp.float32),
            grid_spec=pltpu.PrefetchScalarGridSpec(
                num_scalar_prefetch=1,
                grid=(rows,),
                in_specs=[
                    pl.BlockSpec(
                        (1, n_row, 1, width, s_local),
                        lambda a, ids: ((a + offset) % ratio, 0, (a + offset) // ratio, 0, 0),
                    ),
                    pl.BlockSpec((n_row, blocks_b, width, s_local), lambda a, ids: (0, 0, 0, 0)),
                    pl.BlockSpec(full_row, lambda a, ids: (a + offset, 0, 0, 0, 0, 0)),
                ] + [pl.BlockSpec(memory_space=pl.ANY)] * len(extra),
                out_specs=pl.BlockSpec(full_row, lambda a, ids: (a + offset, 0, 0, 0, 0, 0)),
            ),
            input_output_aliases={} if prev is None else {4: 0},
            compiler_params=pltpu.CompilerParams(vmem_limit_bytes=48 * 1024 * 1024),
        )(ids, row5, col_t, covariance, *extra)

    refreshed = refresh_half(0, half, None)
    refreshed = refresh_half(half, blocks_a - half, refreshed)

    result = pl.pallas_call(
        functools.partial(update_kernel, n_row=n_row, n_col=n_col, blocks_a=blocks_a),
        out_shape=jax.ShapeDtypeStruct(covariance.shape, jnp.float32),
        grid_spec=pltpu.PrefetchScalarGridSpec(
            num_scalar_prefetch=1,
            grid=(blocks_a,),
            in_specs=[
                pl.BlockSpec(full_row, lambda a, ids: (late_pick(a, ids), 0, 0, 0, 0, 0)),
                pl.BlockSpec((1, width, width), lambda a, ids: (late_pick(a, ids), 0, 0)),
                pl.BlockSpec((blocks_b, width, width), lambda a, ids: (0, 0, 0)),
                pl.BlockSpec((width, width), lambda a, ids: (0, 0)),
            ],
            out_specs=pl.BlockSpec(full_row, lambda a, ids: (late_pick(a, ids), 0, 0, 0, 0, 0)),
        ),
        input_output_aliases={1: 0},
        compiler_params=pltpu.CompilerParams(vmem_limit_bytes=48 * 1024 * 1024),
    )(ids, refreshed, panel_rows, panel_cols, factor)
    return result


def solution(mesh):
    n_row = mesh.shape["row"]
    n_col = mesh.shape["col"]
    in_specs = (P(None, "row", None, "col", None, None), P("row", None, "col", None), P(), P())
    out_specs = P(None, "row", None, "col", None, None)
    return jax.shard_map(
        functools.partial(body, n_row=n_row, n_col=n_col),
        mesh=mesh,
        in_specs=in_specs,
        out_specs=out_specs,
        check_vma=False,
    )
```
